1024 devices in a mesh: row: 32 (over x, y_lo), col: 32 (over y_hi, z, core).
Axes of the slice: x: 8, y: 8 (y_hi: 2, y_lo: 4; y = y_hi * 4 + y_lo), z: 8, core: 2. Of those that a mesh axis runs over, the one named last changes fastest.
Arguments:
- basis: bfloat16 [512, 32768], P('row', 'col'), may hold values from -6 to 6
- position: int32 [2, 32768], P(None, 'col'), may hold values from 0 to 65535, as said below
- poles: float32 [65536], P(('row', 'col')), may hold values from 0 to 65536, as said below
- weights: float32 [65536], P(('row', 'col')), may hold values from -2 to 2
- kept: int32 [65536], P(('row', 'col')), may hold values 0 or 1
- eigenvalues: float32 [4096], P('col'), may hold values from 0.5 to 65536, as said below
- scales: float32 [4096], P('col'), may hold values from 0.5 to 2
Outputs:
- vectors: bfloat16 [512, 4096], P('row', 'col')
The draws below stay inside these ranges and needn't reach their ends.
Inputs may be any that keep to these rules, and one draw needn't show every extreme that they name: `position`: each of 0 to 65535 appears once. The poles need not be sorted along the merged order, and every pole's fractional part lies within 0.05 to 0.45. `eigenvalues`: every eigenvalue's fractional part lies within 0.5 to 0.95, so that every eigenvalue stands 0.05 or more away from every pole.
All inputs are finite; a program needn't handle non-finite values. No bound on the sum of `kept` on one device may be relied on, other than what follows from the above.
Results may differ from the reference program's by a relative error of at most 0.0014.
Values may be sent and summed in bfloat16 or wider, within the bound.
No kernel may reach another device: no remote copies, remote signals or barrier semaphores. Data moves between devices by JAX's collectives and lax.ppermute only.
A program may use at most 32 MiB of HBM per device.

```python
import math
import jax
import jax.numpy as jnp
from jax import lax

HALF = 32768
ORDER = 65536
ROWS = 512
NEWCOLS = 4096


def draw_position(key, part):
    order_perm = jax.random.permutation(jax.random.fold_in(key, 11), ORDER)
    return order_perm.astype(jnp.int32).reshape(2, HALF)


def skewed_cells(key, count):
    first_cell = jax.random.randint(jax.random.fold_in(key, 3), (count,), 0, ORDER)
    second_cell = jax.random.randint(jax.random.fold_in(key, 5), (count,), 0, ORDER)
    return jnp.minimum(first_cell, second_cell)


def draw_poles(key, part):
    cell_key = jax.random.fold_in(key, 19)
    sub_key = jax.random.fold_in(key, 23)
    base_cell = skewed_cells(cell_key, ORDER).astype(jnp.float32)
    offsets = jax.random.uniform(sub_key, (ORDER,), jnp.float32, 0.1, 0.4)
    return jnp.sort(base_cell + offsets)


def draw_eigenvalues(key, part):
    first_key = jax.random.fold_in(key, 31)
    second_key = jax.random.fold_in(key, 37)
    base_cell = skewed_cells(first_key, NEWCOLS).astype(jnp.float32)
    fraction = jax.random.uniform(second_key, (NEWCOLS,), jnp.float32, 0.55, 0.95)
    return base_cell + fraction


def with_ends(values, rng, smallest, top_value):
    shape = values.shape
    index_at = [jax.random.randint(jax.random.fold_in(rng, axis), (), 0, shape[axis]) for axis in range(len(shape))]
    values = values.at[tuple(index_at)].set(smallest)
    longest = shape.index(max(shape))
    index_at[longest] = (index_at[longest] + 1) % shape[longest]
    return values.at[tuple(index_at)].set(top_value)


def block_levels(own_key, shape, pieces, smallest, largest):
    gain = 1.0
    for dim, shards_of in pieces:
        steps = jax.random.uniform(jax.random.fold_in(jax.random.fold_in(own_key, 6), dim), (shards_of,), jnp.float32, smallest / len(pieces), largest / len(pieces))
        gain = gain * jnp.repeat(jnp.exp(steps), shape[dim] // shards_of).reshape((-1,) + (1,) * (len(shape) - 1 - dim))
    return gain


def noise(key, shape, width, reach, shards=(), held_as=jnp.bfloat16):
    values = width * jax.random.normal(key, shape, jnp.float32)
    if shards:
        values = values * block_levels(key, shape, shards, -0.22, 0.18)
    return jnp.clip(values, -reach, reach).astype(held_as)


def setup_inputs(seed: int = 0) -> dict:
    splits = jax.random.split(jax.random.key(seed), 8)
    return {
        "basis": noise(splits[0], (ROWS, HALF), 1.0, 6.0, ((0, 32), (1, 32))),
        "position": draw_position(jax.random.fold_in(splits[7], 71), 0),
        "poles": draw_poles(jax.random.fold_in(splits[7], 71), 0),
        "weights": noise(splits[3], (ORDER,), 0.3, 2.0, ((0, 1024),), jnp.float32),
        "kept": with_ends((jax.random.randint(splits[4], (ORDER,), 0, 4) < 3).astype(jnp.int32), jax.random.fold_in(splits[4], 1), 0, 1),
        "eigenvalues": draw_eigenvalues(jax.random.fold_in(splits[7], 71), 0),
        "scales": jnp.clip(jnp.exp(math.log(2.0) - 1.3862944 * jax.random.uniform(splits[6], (NEWCOLS,), jnp.float32) ** block_levels(splits[6], (NEWCOLS,), ((0, 32),), -0.2, 0.2)), 0.5, 2.0),
    }


def split_parts(cauchy):
    upper = cauchy.astype(jnp.bfloat16)
    upper = lax.optimization_barrier(upper)
    lower = (cauchy - upper.astype(jnp.float32)).astype(jnp.bfloat16)
    return upper, lower


def reference(basis, position, poles, weights, kept, eigenvalues, scales):
    live_weight = weights * kept.astype(jnp.float32)
    pole_at = poles[position]
    live_at = live_weight[position]
    child_rows = basis.shape[0] // 2
    stride = math.gcd(eigenvalues.shape[0], 512)

    def column_block(values_pair):
        value_block, scale_block = values_pair
        products = []
        for child_id in range(2):
            cauchy = (live_at[child_id][:, None] / (pole_at[child_id][:, None] - value_block[None, :])) * scale_block[None, :]
            upper, lower = split_parts(cauchy)
            rows_of = basis[child_id * child_rows:(child_id + 1) * child_rows]
            first_term = jnp.dot(rows_of, upper, preferred_element_type=jnp.float32)
            second_term = jnp.dot(rows_of, lower, preferred_element_type=jnp.float32)
            products.append(first_term + second_term)
        return jnp.concatenate(products, axis=0)

    stacked = lax.map(column_block, (eigenvalues.reshape(-1, stride), scales.reshape(-1, stride)))
    result = jnp.transpose(stacked, (1, 0, 2)).reshape(basis.shape[0], eigenvalues.shape[0])
    return result.astype(jnp.bfloat16)
```

```python
import math

import jax
import jax.numpy as jnp
from jax import lax
from jax.sharding import PartitionSpec as P


def split_parts(cauchy):
    upper = cauchy.astype(jnp.bfloat16)
    upper = lax.optimization_barrier(upper)
    lower = (cauchy - upper.astype(jnp.float32)).astype(jnp.bfloat16)
    return (upper, lower)


def cauchy_tile(pole_at, live_at, value_row, scale_row):
    return live_at[:, None] / (pole_at[:, None] - value_row[None, :]) * scale_row[None, :]


def per_device(basis, position, poles, weights, kept, eigenvalues, scales):
    live_weight = weights * kept.astype(jnp.float32)
    pole_data = lax.all_gather(jnp.stack([poles, live_weight]), "col", axis=1, tiled=True)
    pole_data = lax.all_gather(pole_data, "row", axis=1, tiled=True)
    row_total = lax.axis_size("row")
    child_id = lax.axis_index("row") // (row_total // 2)
    own_index = lax.dynamic_index_in_dim(position, child_id, 0, keepdims=False)
    own_poles = jnp.stack([pole_data[0][own_index], pole_data[1][own_index]])
    child_poles = lax.all_gather(own_poles, "col", axis=1, tiled=True)
    rows_dev = basis.shape[0]
    cols_dev = eigenvalues.shape[0]
    zeros_init = jnp.zeros((rows_dev, cols_dev), jnp.float32)
    columns_in = lax.all_gather(basis, "col", axis=1, tiled=True)
    span_cols = columns_in.shape[1]
    stride = math.gcd(span_cols, 4096)

    def add_block(block_id, partial_sum):
        offset = block_id * stride
        cols_block = lax.dynamic_slice_in_dim(columns_in, offset, stride, 1)
        poles_block = lax.dynamic_slice_in_dim(child_poles, offset, stride, 1)
        upper, lower = split_parts(cauchy_tile(poles_block[0], poles_block[1], eigenvalues, scales))
        first_term = jnp.dot(cols_block, upper, preferred_element_type=jnp.float32)
        second_term = jnp.dot(cols_block, lower, preferred_element_type=jnp.float32)
        return partial_sum + (first_term + second_term)

    summed = lax.fori_loop(0, span_cols // stride, add_block, zeros_init)
    return summed.astype(jnp.bfloat16)


def solution(mesh):
    placed = (
        P("row", "col"),
        P(None, "col"),
        P(("row", "col")),
        P(("row", "col")),
        P(("row", "col")),
        P("col"),
        P("col"),
    )
    return jax.shard_map(
        per_device, mesh=mesh, in_specs=placed, out_specs=P("row", "col"), check_vma=False
    )
```

```python
import jax
import jax.numpy as jnp
from jax import lax
from jax.sharding import PartitionSpec as P


def split_parts(cauchy):
    upper = cauchy.astype(jnp.bfloat16)
    upper = lax.optimization_barrier(upper)
    lower = (cauchy - upper.astype(jnp.float32)).astype(jnp.bfloat16)
    return (upper, lower)


def cauchy_tile(pole_at, live_at, value_row, scale_row):
    return live_at[:, None] / (pole_at[:, None] - value_row[None, :]) * scale_row[None, :]


def per_device(basis, position, poles, weights, kept, eigenvalues, scales):
    live_weight = weights * kept.astype(jnp.float32)
    pole_data = lax.all_gather(jnp.stack([poles, live_weight]), "col", axis=1, tiled=True)
    pole_data = lax.all_gather(pole_data, "row", axis=1, tiled=True)
    row_total = lax.axis_size("row")
    child_id = lax.axis_index("row") // (row_total // 2)
    own_index = lax.dynamic_index_in_dim(position, child_id, 0, keepdims=False)
    pole_at = pole_data[0][own_index]
    live_at = pole_data[1][own_index]
    value_data = lax.all_gather(jnp.stack([eigenvalues, scales]), "col", axis=1, tiled=True)
    span_new = value_data.shape[1]
    stride = 512

    def add_block(block_id, partial):
        offset = block_id * stride
        values = lax.dynamic_slice_in_dim(value_data, offset, stride, 1)
        upper, lower = split_parts(cauchy_tile(pole_at, live_at, values[0], values[1]))
        first_term = jnp.dot(basis, upper, preferred_element_type=jnp.float32)
        second_term = jnp.dot(basis, lower, preferred_element_type=jnp.float32)
        return lax.dynamic_update_slice_in_dim(partial, first_term + second_term, offset, 1)

    partial = jnp.zeros((basis.shape[0], span_new), jnp.float32)
    partial = lax.fori_loop(0, span_new // stride, add_block, partial)
    summed = lax.psum_scatter(partial, "col", scatter_dimension=1, tiled=True)
    return summed.astype(jnp.bfloat16)


def solution(mesh):
    placed = (
        P("row", "col"),
        P(None, "col"),
        P(("row", "col")),
        P(("row", "col")),
        P(("row", "col")),
        P("col"),
        P("col"),
    )
    return jax.shard_map(
        per_device, mesh=mesh, in_specs=placed, out_specs=P("row", "col"), check_vma=False
    )
```

```python
import math

import jax
import jax.numpy as jnp
from jax import lax
from jax.sharding import PartitionSpec as P


def split_parts(cauchy):
    upper = cauchy.astype(jnp.bfloat16)
    upper = lax.optimization_barrier(upper)
    lower = (cauchy - upper.astype(jnp.float32)).astype(jnp.bfloat16)
    return (upper, lower)


def cauchy_tile(pole_at, live_at, value_row, scale_row):
    return live_at[:, None] / (pole_at[:, None] - value_row[None, :]) * scale_row[None, :]


def gather_by_pairs(block, axis):
    size = lax.axis_size(axis)
    index = lax.axis_index(axis)
    held = block
    step = 1
    while step < size:
        other = lax.ppermute(held, axis, perm=[(i, i ^ step) for i in range(size)])
        low_half = (index // step) % 2 == 0
        held = jnp.where(low_half, jnp.concatenate([held, other], -1), jnp.concatenate([other, held], -1))
        step *= 2
    return held


def per_device(basis, position, poles, weights, kept, eigenvalues, scales):
    live_weight = weights * kept.astype(jnp.float32)
    pole_data = gather_by_pairs(jnp.stack([poles, live_weight]), "col")
    pole_data = gather_by_pairs(pole_data, "row")
    row_total = lax.axis_size("row")
    child_id = lax.axis_index("row") // (row_total // 2)
    own_index = lax.dynamic_index_in_dim(position, child_id, 0, keepdims=False)
    own_poles = jnp.stack([pole_data[0][own_index], pole_data[1][own_index]])
    child_poles = gather_by_pairs(own_poles, "col")
    rows_dev = basis.shape[0]
    cols_dev = eigenvalues.shape[0]
    zeros_init = jnp.zeros((rows_dev, cols_dev), jnp.float32)
    columns_in = lax.all_gather(basis, "col", axis=1, tiled=True)
    span_cols = columns_in.shape[1]
    stride = math.gcd(span_cols, 4096)

    def add_block(block_id, partial_sum):
        offset = block_id * stride
        cols_block = lax.dynamic_slice_in_dim(columns_in, offset, stride, 1)
        poles_block = lax.dynamic_slice_in_dim(child_poles, offset, stride, 1)
        upper, lower = split_parts(cauchy_tile(poles_block[0], poles_block[1], eigenvalues, scales))
        first_term = jnp.dot(cols_block, upper, preferred_element_type=jnp.float32)
        second_term = jnp.dot(cols_block, lower, preferred_element_type=jnp.float32)
        return partial_sum + (first_term + second_term)

    summed = lax.fori_loop(0, span_cols // stride, add_block, zeros_init)
    return summed.astype(jnp.bfloat16)


def solution(mesh):
    placed = (
        P("row", "col"),
        P(None, "col"),
        P(("row", "col")),
        P(("row", "col")),
        P(("row", "col")),
        P("col"),
        P("col"),
    )
    return jax.shard_map(
        per_device, mesh=mesh, in_specs=placed, out_specs=P("row", "col"), check_vma=False
    )
```

```python
import math

import jax
import jax.numpy as jnp
from jax import lax
from jax.sharding import PartitionSpec as P


def split_parts(cauchy):
    upper = cauchy.astype(jnp.bfloat16)
    upper = lax.optimization_barrier(upper)
    lower = (cauchy - upper.astype(jnp.float32)).astype(jnp.bfloat16)
    return (upper, lower)


def cauchy_tile_t(pole_row, live_row, value_at, scale_at):
    return live_row[None, :] / (pole_row[None, :] - value_at[:, None]) * scale_at[:, None]


def gather_by_pairs(block, axis):
    size = lax.axis_size(axis)
    index = lax.axis_index(axis)
    held = block
    step = 1
    while step < size:
        other = lax.ppermute(held, axis, perm=[(i, i ^ step) for i in range(size)])
        low_half = (index // step) % 2 == 0
        held = jnp.where(low_half, jnp.concatenate([held, other], -1), jnp.concatenate([other, held], -1))
        step *= 2
    return held


def per_device(basis, position, poles, weights, kept, eigenvalues, scales):
    live_weight = weights * kept.astype(jnp.float32)
    pole_data = gather_by_pairs(jnp.stack([poles, live_weight]), "col")
    pole_data = gather_by_pairs(pole_data, "row")
    columns_in = gather_by_pairs(basis, "col")
    pole_data, columns_in = lax.optimization_barrier((pole_data, columns_in))
    row_total = lax.axis_size("row")
    child_id = lax.axis_index("row") // (row_total // 2)
    own_index = lax.dynamic_index_in_dim(position, child_id, 0, keepdims=False)
    own_poles = jnp.stack([pole_data[0][own_index], pole_data[1][own_index]])
    child_poles = gather_by_pairs(own_poles, "col")
    rows_dev = basis.shape[0]
    cols_dev = eigenvalues.shape[0]
    zeros_init = jnp.zeros((rows_dev, cols_dev), jnp.float32)
    span_cols = columns_in.shape[1]
    stride = math.gcd(span_cols, 4096)

    def add_block(block_id, partial_sum):
        offset = block_id * stride
        cols_block = lax.dynamic_slice_in_dim(columns_in, offset, stride, 1)
        poles_block = lax.dynamic_slice_in_dim(child_poles, offset, stride, 1)
        upper, lower = split_parts(cauchy_tile_t(poles_block[0], poles_block[1], eigenvalues, scales))
        contract = (((1,), (1,)), ((), ()))
        first_term = lax.dot_general(cols_block, upper, contract, preferred_element_type=jnp.float32)
        second_term = lax.dot_general(cols_block, lower, contract, preferred_element_type=jnp.float32)
        return partial_sum + (first_term + second_term)

    summed = lax.fori_loop(0, span_cols // stride, add_block, zeros_init)
    return summed.astype(jnp.bfloat16)


def solution(mesh):
    placed = (
        P("row", "col"),
        P(None, "col"),
        P(("row", "col")),
        P(("row", "col")),
        P(("row", "col")),
        P("col"),
        P("col"),
    )
    return jax.shard_map(
        per_device, mesh=mesh, in_specs=placed, out_specs=P("row", "col"), check_vma=False
    )
```

```python
import math

import jax
import jax.numpy as jnp
from jax import lax
from jax.sharding import PartitionSpec as P


def split_parts(cauchy):
    upper = cauchy.astype(jnp.bfloat16)
    upper = lax.optimization_barrier(upper)
    lower = (cauchy - upper.astype(jnp.float32)).astype(jnp.bfloat16)
    return (upper, lower)


def cauchy_tile_t(pole_row, live_row, value_at, scale_at):
    return live_row[None, :] / (pole_row[None, :] - value_at[:, None]) * scale_at[:, None]


def gather_by_pairs(block, axis):
    size = lax.axis_size(axis)
    index = lax.axis_index(axis)
    held = block
    step = 1
    while step < size:
        other = lax.ppermute(held, axis, perm=[(i, i ^ step) for i in range(size)])
        low_half = (index // step) % 2 == 0
        held = jnp.where(low_half, jnp.concatenate([held, other], -1), jnp.concatenate([other, held], -1))
        step *= 2
    return held


def per_device(basis, position, poles, weights, kept, eigenvalues, scales):
    live_weight = weights * kept.astype(jnp.float32)
    pole_data = gather_by_pairs(jnp.stack([poles, live_weight]), "col")
    pole_data = gather_by_pairs(pole_data, "row")
    columns_in = gather_by_pairs(basis, "col")
    pole_data, columns_in = lax.optimization_barrier((pole_data, columns_in))
    row_total = lax.axis_size("row")
    child_id = lax.axis_index("row") // (row_total // 2)
    own_index = lax.dynamic_index_in_dim(position, child_id, 0, keepdims=False)
    held = jnp.stack([pole_data[0][own_index], pole_data[1][own_index]])
    rows_dev = basis.shape[0]
    cols_dev = eigenvalues.shape[0]
    own_cols = held.shape[1]
    col_total = lax.axis_size("col")
    col_index = lax.axis_index("col")
    tile = 4096
    contract = (((1,), (1,)), ((), ()))

    def add_tile(partial_sum, cols_block, poles_block):
        upper, lower = split_parts(cauchy_tile_t(poles_block[0], poles_block[1], eigenvalues, scales))
        first_term = lax.dot_general(cols_block, upper, contract, preferred_element_type=jnp.float32)
        second_term = lax.dot_general(cols_block, lower, contract, preferred_element_type=jnp.float32)
        return partial_sum + (first_term + second_term)

    def add_range(partial_sum, values, offset):
        length = values.shape[1]
        if length <= tile:
            cols_block = lax.dynamic_slice_in_dim(columns_in, offset, length, 1)
            return add_tile(partial_sum, cols_block, values)

        def add_block(block_id, acc):
            start = block_id * tile
            cols_block = lax.dynamic_slice_in_dim(columns_in, offset + start, tile, 1)
            poles_block = lax.dynamic_slice_in_dim(values, start, tile, 1)
            return add_tile(acc, cols_block, poles_block)

        return lax.fori_loop(0, length // tile, add_block, partial_sum)

    summed = add_range(jnp.zeros((rows_dev, cols_dev), jnp.float32), held, col_index * own_cols)
    step = 1
    while step < col_total:
        other = lax.ppermute(held, "col", perm=[(i, i ^ step) for i in range(col_total)])
        other_at = ((col_index // step) ^ 1) * step * own_cols
        summed = add_range(summed, other, other_at)
        if step * 2 < col_total:
            low_half = (col_index // step) % 2 == 0
            held = jnp.where(low_half, jnp.concatenate([held, other], -1), jnp.concatenate([other, held], -1))
        step *= 2
    return summed.astype(jnp.bfloat16)


def solution(mesh):
    placed = (
        P("row", "col"),
        P(None, "col"),
        P(("row", "col")),
        P(("row", "col")),
        P(("row", "col")),
        P("col"),
        P("col"),
    )
    return jax.shard_map(
        per_device, mesh=mesh, in_specs=placed, out_specs=P("row", "col"), check_vma=False
    )
```

```python
import jax
import jax.numpy as jnp
from jax import lax
from jax.sharding import PartitionSpec as P


def split_parts(cauchy):
    upper = cauchy.astype(jnp.bfloat16)
    upper = lax.optimization_barrier(upper)
    lower = (cauchy - upper.astype(jnp.float32)).astype(jnp.bfloat16)
    return (upper, lower)


def cauchy_tile_t(pole_row, live_row, value_at, scale_at):
    return live_row[None, :] / (pole_row[None, :] - value_at[:, None]) * scale_at[:, None]


def gather_by_pairs(block, axis):
    size = lax.axis_size(axis)
    index = lax.axis_index(axis)
    held = block
    step = 1
    while step < size:
        other = lax.ppermute(held, axis, perm=[(i, i ^ step) for i in range(size)])
        low_half = (index // step) % 2 == 0
        held = jnp.where(low_half, jnp.concatenate([held, other], -1), jnp.concatenate([other, held], -1))
        step *= 2
    return held


def reduce_by_halves(compute_range, total, axis):
    size = lax.axis_size(axis)
    index = lax.axis_index(axis)
    step = size // 2
    width = total // 2
    bit = (index // step) % 2
    sent = compute_range((1 - bit) * width, width)
    got = lax.ppermute(sent, axis, perm=[(i, i ^ step) for i in range(size)])
    held = compute_range(bit * width, width) + got
    step //= 2
    while step >= 1:
        width //= 2
        bit = (index // step) % 2
        sent = lax.dynamic_slice_in_dim(held, (1 - bit) * width, width, -1)
        kept = lax.dynamic_slice_in_dim(held, bit * width, width, -1)
        held = kept + lax.ppermute(sent, axis, perm=[(i, i ^ step) for i in range(size)])
        step //= 2
    return held


def per_device(basis, position, poles, weights, kept, eigenvalues, scales):
    live_weight = weights * kept.astype(jnp.float32)
    col_total = lax.axis_size("col")
    pole_dev = poles.shape[0]
    both = jnp.concatenate([jnp.stack([poles, live_weight]), jnp.stack([eigenvalues, scales])], 1)
    both = gather_by_pairs(both, "col").reshape(2, col_total, -1)
    pole_data = both[:, :, :pole_dev].reshape(2, -1)
    value_data = both[:, :, pole_dev:].reshape(2, -1)
    pole_data = gather_by_pairs(pole_data, "row")
    row_total = lax.axis_size("row")
    child_id = lax.axis_index("row") // (row_total // 2)
    own_index = lax.dynamic_index_in_dim(position, child_id, 0, keepdims=False)
    pole_at = pole_data[0][own_index]
    live_at = pole_data[1][own_index]
    chunk = 512
    contract = (((1,), (1,)), ((), ()))

    def compute_range(offset, width):
        parts = []
        for start in range(0, width, chunk):
            values = lax.dynamic_slice_in_dim(value_data, offset + start, chunk, 1)
            upper, lower = split_parts(cauchy_tile_t(pole_at, live_at, values[0], values[1]))
            first_term = lax.dot_general(basis, upper, contract, preferred_element_type=jnp.float32)
            second_term = lax.dot_general(basis, lower, contract, preferred_element_type=jnp.float32)
            parts.append(first_term + second_term)
        return jnp.concatenate(parts, 1)

    summed = reduce_by_halves(compute_range, value_data.shape[1], "col")
    return summed.astype(jnp.bfloat16)


def solution(mesh):
    placed = (
        P("row", "col"),
        P(None, "col"),
        P(("row", "col")),
        P(("row", "col")),
        P(("row", "col")),
        P("col"),
        P("col"),
    )
    return jax.shard_map(
        per_device, mesh=mesh, in_specs=placed, out_specs=P("row", "col"), check_vma=False
    )
```

```python
import jax
import jax.numpy as jnp
from jax import lax
from jax.sharding import PartitionSpec as P


def split_parts(cauchy):
    upper = cauchy.astype(jnp.bfloat16)
    upper = lax.optimization_barrier(upper)
    lower = (cauchy - upper.astype(jnp.float32)).astype(jnp.bfloat16)
    return (upper, lower)


def cauchy_tile_t(pole_row, live_row, value_at, scale_at):
    return live_row[None, :] / (pole_row[None, :] - value_at[:, None]) * scale_at[:, None]


def gather_by_pairs(block, axis):
    size = lax.axis_size(axis)
    index = lax.axis_index(axis)
    held = block
    step = 1
    while step < size:
        other = lax.ppermute(held, axis, perm=[(i, i ^ step) for i in range(size)])
        low_half = (index // step) % 2 == 0
        held = jnp.where(low_half, jnp.concatenate([held, other], -1), jnp.concatenate([other, held], -1))
        step *= 2
    return held


def reduce_by_halves(compute_range, total, axis):
    size = lax.axis_size(axis)
    index = lax.axis_index(axis)
    step = size // 2
    width = total // 2
    bit = (index // step) % 2
    sent = compute_range((1 - bit) * width, width)
    got = lax.ppermute(sent, axis, perm=[(i, i ^ step) for i in range(size)])
    held = compute_range(bit * width, width) + got
    step //= 2
    while step >= 1:
        width //= 2
        bit = (index // step) % 2
        sent = lax.dynamic_slice_in_dim(held, (1 - bit) * width, width, -1)
        kept = lax.dynamic_slice_in_dim(held, bit * width, width, -1)
        held = kept + lax.ppermute(sent, axis, perm=[(i, i ^ step) for i in range(size)])
        step //= 2
    return held


def per_device(basis, position, poles, weights, kept, eigenvalues, scales):
    live_weight = weights * kept.astype(jnp.float32)
    col_total = lax.axis_size("col")
    pole_dev = poles.shape[0]
    both = jnp.concatenate([jnp.stack([poles, live_weight]), jnp.stack([eigenvalues, scales])], 1)
    both = gather_by_pairs(both, "col").reshape(2, col_total, -1)
    pole_part = both[:, :, :pole_dev].reshape(2, -1)
    value_data = both[:, :, pole_dev:].reshape(2, -1)
    part_len = pole_part.shape[1]
    base = lax.axis_index("row") * part_len
    pieces = []
    rest = pole_part
    for _ in range(3):
        piece = lax.optimization_barrier(rest.astype(jnp.bfloat16))
        rest = rest - piece.astype(jnp.float32)
        pieces.append(piece)
    table = jnp.concatenate(pieces, 0)
    local = position.reshape(-1) - base
    looked = []
    span = 512
    for start in range(0, local.shape[0], span):
        hits = local[start:start + span, None] == lax.iota(jnp.int32, part_len)[None, :]
        found = lax.dot_general(table, hits.astype(jnp.bfloat16), (((1,), (1,)), ((), ())), preferred_element_type=jnp.float32)
        looked.append((found[0:2] + found[2:4]) + found[4:6])
    looked = jnp.concatenate(looked, 1)
    row_total = lax.axis_size("row")
    step = 1
    while step < row_total:
        looked = looked + lax.ppermute(looked, "row", perm=[(i, i ^ step) for i in range(row_total)])
        step *= 2
    child_id = lax.axis_index("row") // (row_total // 2)
    own_cols = position.shape[1]
    own_poles = lax.dynamic_slice_in_dim(looked, child_id * own_cols, own_cols, 1)
    pole_at = own_poles[0]
    live_at = own_poles[1]
    chunk = 512
    contract = (((1,), (1,)), ((), ()))

    def compute_range(offset, width):
        parts = []
        for start in range(0, width, chunk):
            values = lax.dynamic_slice_in_dim(value_data, offset + start, chunk, 1)
            upper, lower = split_parts(cauchy_tile_t(pole_at, live_at, values[0], values[1]))
            first_term = lax.dot_general(basis, upper, contract, preferred_element_type=jnp.float32)
            second_term = lax.dot_general(basis, lower, contract, preferred_element_type=jnp.float32)
            parts.append(first_term + second_term)
        return jnp.concatenate(parts, 1)

    summed = reduce_by_halves(compute_range, value_data.shape[1], "col")
    return summed.astype(jnp.bfloat16)


def solution(mesh):
    placed = (
        P("row", "col"),
        P(None, "col"),
        P(("row", "col")),
        P(("row", "col")),
        P(("row", "col")),
        P("col"),
        P("col"),
    )
    return jax.shard_map(
        per_device, mesh=mesh, in_specs=placed, out_specs=P("row", "col"), check_vma=False
    )
```

```python
import jax
import jax.numpy as jnp
from jax import lax
from jax.sharding import PartitionSpec as P


def split_parts(cauchy):
    upper = cauchy.astype(jnp.bfloat16)
    upper = lax.optimization_barrier(upper)
    lower = (cauchy - upper.astype(jnp.float32)).astype(jnp.bfloat16)
    return (upper, lower)


def cauchy_tile_t(pole_row, live_row, value_at, scale_at):
    return live_row[None, :] / (pole_row[None, :] - value_at[:, None]) * scale_at[:, None]


def gather_by_pairs(block, axis):
    size = lax.axis_size(axis)
    index = lax.axis_index(axis)
    held = block
    step = 1
    while step < size:
        other = lax.ppermute(held, axis, perm=[(i, i ^ step) for i in range(size)])
        low_half = (index // step) % 2 == 0
        held = jnp.where(low_half, jnp.concatenate([held, other], -1), jnp.concatenate([other, held], -1))
        step *= 2
    return held


def reduce_by_halves(compute_range, total, axis, inputs):
    size = lax.axis_size(axis)
    index = lax.axis_index(axis)
    step = 1
    width = total // 2
    bit = index % 2
    sent = compute_range(inputs, (1 - bit) * width, width)
    sent, inputs = lax.optimization_barrier((sent, inputs))
    got = lax.ppermute(sent, axis, perm=[(i, i ^ step) for i in range(size)])
    held = compute_range(inputs, bit * width, width) + got
    step *= 2
    while step < size:
        width //= 2
        bit = (index // step) % 2
        sent = lax.dynamic_slice_in_dim(held, (1 - bit) * width, width, -1)
        kept = lax.dynamic_slice_in_dim(held, bit * width, width, -1)
        held = kept + lax.ppermute(sent, axis, perm=[(i, i ^ step) for i in range(size)])
        step *= 2
    return held


def bit_reversed(count):
    width = count.bit_length() - 1
    return [int(format(i, "0%db" % width)[::-1], 2) for i in range(count)]


def per_device(basis, position, poles, weights, kept, eigenvalues, scales):
    live_weight = weights * kept.astype(jnp.float32)
    col_total = lax.axis_size("col")
    pole_dev = poles.shape[0]
    both = jnp.concatenate([jnp.stack([poles, live_weight]), jnp.stack([eigenvalues, scales])], 1)
    both = gather_by_pairs(both, "col").reshape(2, col_total, -1)
    pole_part = both[:, :, :pole_dev].reshape(2, -1)
    value_data = both[:, :, pole_dev:].reshape(2, -1)
    part_len = pole_part.shape[1]
    base = lax.axis_index("row") * part_len
    pieces = []
    rest = pole_part
    for _ in range(3):
        piece = lax.optimization_barrier(rest.astype(jnp.bfloat16))
        rest = rest - piece.astype(jnp.float32)
        pieces.append(piece)
    table = jnp.concatenate(pieces, 0)
    local = position.reshape(-1) - base
    looked = []
    span = 512
    for start in range(0, local.shape[0], span):
        hits = local[start:start + span, None] == lax.iota(jnp.int32, part_len)[None, :]
        found = lax.dot_general(table, hits.astype(jnp.bfloat16), (((1,), (1,)), ((), ())), preferred_element_type=jnp.float32)
        looked.append((found[0:2] + found[2:4]) + found[4:6])
    looked = jnp.concatenate(looked, 1)
    row_total = lax.axis_size("row")
    step = 1
    while step < row_total:
        looked = looked + lax.ppermute(looked, "row", perm=[(i, i ^ step) for i in range(row_total)])
        step *= 2
    child_id = lax.axis_index("row") // (row_total // 2)
    own_cols = position.shape[1]
    own_poles = lax.dynamic_slice_in_dim(looked, child_id * own_cols, own_cols, 1)
    pole_at = own_poles[0]
    live_at = own_poles[1]
    chunk = 512
    contract = (((1,), (1,)), ((), ()))

    blocks = value_data.reshape(2, col_total, -1)
    value_data = jnp.concatenate([blocks[:, b] for b in bit_reversed(col_total)], 1)

    def compute_range(inputs, offset, width):
        pole_at, live_at, value_data = inputs
        parts = []
        for start in range(0, width, chunk):
            values = lax.dynamic_slice_in_dim(value_data, offset + start, chunk, 1)
            upper, lower = split_parts(cauchy_tile_t(pole_at, live_at, values[0], values[1]))
            first_term = lax.dot_general(basis, upper, contract, preferred_element_type=jnp.float32)
            second_term = lax.dot_general(basis, lower, contract, preferred_element_type=jnp.float32)
            parts.append(first_term + second_term)
        return jnp.concatenate(parts, 1)

    summed = reduce_by_halves(compute_range, value_data.shape[1], "col", (pole_at, live_at, value_data))
    return summed.astype(jnp.bfloat16)


def solution(mesh):
    placed = (
        P("row", "col"),
        P(None, "col"),
        P(("row", "col")),
        P(("row", "col")),
        P(("row", "col")),
        P("col"),
        P("col"),
    )
    return jax.shard_map(
        per_device, mesh=mesh, in_specs=placed, out_specs=P("row", "col"), check_vma=False
    )
```

```python
import jax
import jax.numpy as jnp
from jax import lax
from jax.sharding import PartitionSpec as P


def split_parts(cauchy):
    upper = cauchy.astype(jnp.bfloat16)
    upper = lax.optimization_barrier(upper)
    lower = (cauchy - upper.astype(jnp.float32)).astype(jnp.bfloat16)
    return (upper, lower)


def cauchy_tile_t(pole_row, live_row, value_at, scale_at):
    return live_row[None, :] / (pole_row[None, :] - value_at[:, None]) * scale_at[:, None]


def gather_by_pairs(block, axis):
    size = lax.axis_size(axis)
    index = lax.axis_index(axis)
    held = block
    step = 1
    while step < size:
        other = lax.ppermute(held, axis, perm=[(i, i ^ step) for i in range(size)])
        low_half = (index // step) % 2 == 0
        held = jnp.where(low_half, jnp.concatenate([held, other], -1), jnp.concatenate([other, held], -1))
        step *= 2
    return held


def reduce_by_halves(compute_range, total, axis, inputs):
    size = lax.axis_size(axis)
    index = lax.axis_index(axis)
    step = 1
    width = total // 2
    bit = index % 2
    sent = compute_range(inputs, (1 - bit) * width, width)
    sent, inputs = lax.optimization_barrier((sent, inputs))
    got = lax.ppermute(sent, axis, perm=[(i, i ^ step) for i in range(size)])
    held = compute_range(inputs, bit * width, width) + got
    step *= 2
    while step < size:
        width //= 2
        bit = (index // step) % 2
        sent = lax.dynamic_slice_in_dim(held, (1 - bit) * width, width, -1)
        kept = lax.dynamic_slice_in_dim(held, bit * width, width, -1)
        held = kept + lax.ppermute(sent, axis, perm=[(i, i ^ step) for i in range(size)])
        step *= 2
    return held


def bit_reversed(count):
    width = count.bit_length() - 1
    return [int(format(i, "0%db" % width)[::-1], 2) for i in range(count)]


def per_device(basis, position, poles, weights, kept, eigenvalues, scales):
    live_weight = weights * kept.astype(jnp.float32)
    col_total = lax.axis_size("col")
    pole_dev = poles.shape[0]
    own = jnp.concatenate([jnp.stack([poles, live_weight]), jnp.stack([eigenvalues, scales])], 1)
    own_len = own.shape[1]
    col_index = lax.axis_index("col")
    row_base = lax.axis_index("row") * (col_total * pole_dev)
    wanted = position.reshape(-1)

    def look_up(block, first_col):
        count = block.shape[1] // own_len
        part = block.reshape(2, count, own_len)[:, :, :pole_dev].reshape(2, -1)
        pieces = []
        rest = part
        for _ in range(3):
            piece = lax.optimization_barrier(rest.astype(jnp.bfloat16))
            rest = rest - piece.astype(jnp.float32)
            pieces.append(piece)
        table = jnp.concatenate(pieces, 0)
        local = wanted - (row_base + first_col * pole_dev)
        found_all = []
        span = 512
        for begin in range(0, local.shape[0], span):
            hits = local[begin:begin + span, None] == lax.iota(jnp.int32, part.shape[1])[None, :]
            found = lax.dot_general(table, hits.astype(jnp.bfloat16), (((1,), (1,)), ((), ())), preferred_element_type=jnp.float32)
            found_all.append((found[0:2] + found[2:4]) + found[4:6])
        return jnp.concatenate(found_all, 1)

    looked = look_up(own, col_index)
    held = own
    step = 1
    while step < col_total:
        other = lax.ppermute(held, "col", perm=[(i, i ^ step) for i in range(col_total)])
        looked = looked + look_up(other, ((col_index // step) ^ 1) * step)
        low_half = (col_index // step) % 2 == 0
        held = jnp.where(low_half, jnp.concatenate([held, other], -1), jnp.concatenate([other, held], -1))
        step *= 2
    value_data = held.reshape(2, col_total, own_len)[:, :, pole_dev:].reshape(2, -1)
    row_total = lax.axis_size("row")
    step = 1
    while step < row_total:
        looked = looked + lax.ppermute(looked, "row", perm=[(i, i ^ step) for i in range(row_total)])
        step *= 2
    child_id = lax.axis_index("row") // (row_total // 2)
    own_cols = position.shape[1]
    own_poles = lax.dynamic_slice_in_dim(looked, child_id * own_cols, own_cols, 1)
    pole_at = own_poles[0]
    live_at = own_poles[1]
    chunk = 512
    contract = (((1,), (1,)), ((), ()))

    blocks = value_data.reshape(2, col_total, -1)
    value_data = jnp.concatenate([blocks[:, b] for b in bit_reversed(col_total)], 1)

    def compute_range(inputs, offset, width):
        pole_at, live_at, value_data = inputs
        parts = []
        for start in range(0, width, chunk):
            values = lax.dynamic_slice_in_dim(value_data, offset + start, chunk, 1)
            upper, lower = split_parts(cauchy_tile_t(pole_at, live_at, values[0], values[1]))
            first_term = lax.dot_general(basis, upper, contract, preferred_element_type=jnp.float32)
            second_term = lax.dot_general(basis, lower, contract, preferred_element_type=jnp.float32)
            parts.append(first_term + second_term)
        return jnp.concatenate(parts, 1)

    summed = reduce_by_halves(compute_range, value_data.shape[1], "col", (pole_at, live_at, value_data))
    return summed.astype(jnp.bfloat16)


def solution(mesh):
    placed = (
        P("row", "col"),
        P(None, "col"),
        P(("row", "col")),
        P(("row", "col")),
        P(("row", "col")),
        P("col"),
        P("col"),
    )
    return jax.shard_map(
        per_device, mesh=mesh, in_specs=placed, out_specs=P("row", "col"), check_vma=False
    )
```

```python
import jax
import jax.numpy as jnp
from jax import lax
from jax.sharding import PartitionSpec as P


def split_parts(cauchy):
    upper = cauchy.astype(jnp.bfloat16)
    upper = lax.optimization_barrier(upper)
    lower = (cauchy - upper.astype(jnp.float32)).astype(jnp.bfloat16)
    return (upper, lower)


def cauchy_tile_t(pole_row, live_row, value_at, scale_at):
    return live_row[None, :] / (pole_row[None, :] - value_at[:, None]) * scale_at[:, None]


def gather_by_pairs(block, axis):
    size = lax.axis_size(axis)
    index = lax.axis_index(axis)
    held = block
    step = 1
    while step < size:
        other = lax.ppermute(held, axis, perm=[(i, i ^ step) for i in range(size)])
        low_half = (index // step) % 2 == 0
        held = jnp.where(low_half, jnp.concatenate([held, other], -1), jnp.concatenate([other, held], -1))
        step *= 2
    return held


def reduce_by_halves(compute_range, first_offset, total, axis, inputs, step):
    size = lax.axis_size(axis)
    index = lax.axis_index(axis)
    width = total // 2
    bit = (index // step) % 2
    sent = compute_range(inputs, first_offset + (1 - bit) * width, width)
    sent, inputs = lax.optimization_barrier((sent, inputs))
    got = lax.ppermute(sent, axis, perm=[(i, i ^ step) for i in range(size)])
    held = compute_range(inputs, first_offset + bit * width, width) + got
    step *= 2
    while step < size:
        width //= 2
        bit = (index // step) % 2
        sent = lax.dynamic_slice_in_dim(held, (1 - bit) * width, width, -1)
        kept = lax.dynamic_slice_in_dim(held, bit * width, width, -1)
        held = kept + lax.ppermute(sent, axis, perm=[(i, i ^ step) for i in range(size)])
        step *= 2
    return held


def bit_reversed(count):
    width = count.bit_length() - 1
    return [int(format(i, "0%db" % width)[::-1], 2) for i in range(count)]


def per_device(basis, position, poles, weights, kept, eigenvalues, scales):
    live_weight = weights * kept.astype(jnp.float32)
    col_total = lax.axis_size("col")
    pole_dev = poles.shape[0]
    own = jnp.concatenate([jnp.stack([poles, live_weight]), jnp.stack([eigenvalues, scales])], 1)
    own_len = own.shape[1]
    col_index = lax.axis_index("col")
    row_base = lax.axis_index("row") * (col_total * pole_dev)

    def look_up(block, first_col):
        count = block.shape[1] // own_len
        part = block.reshape(2, count, own_len)[:, :, :pole_dev].reshape(2, -1)
        pieces = []
        rest = part
        for _ in range(3):
            piece = lax.optimization_barrier(rest.astype(jnp.bfloat16))
            rest = rest - piece.astype(jnp.float32)
            pieces.append(piece)
        table = jnp.concatenate(pieces, 0)
        local = wanted - (row_base + first_col * pole_dev)
        found_all = []
        span = 512
        for begin in range(0, local.shape[0], span):
            hits = local[begin:begin + span, None] == lax.iota(jnp.int32, part.shape[1])[None, :]
            found = lax.dot_general(table, hits.astype(jnp.bfloat16), (((1,), (1,)), ((), ())), preferred_element_type=jnp.float32)
            found_all.append((found[0:2] + found[2:4]) + found[4:6])
        return jnp.concatenate(found_all, 1)

    pos_len = position.size
    sent = jnp.concatenate([own.reshape(-1), position.astype(jnp.float32).reshape(-1), basis.astype(jnp.float32).reshape(-1)])
    got = lax.ppermute(sent, "col", perm=[(i, i ^ 1) for i in range(col_total)])
    other = got[:own.size].reshape(own.shape)
    mate_position = got[own.size:own.size + pos_len].reshape(position.shape).astype(jnp.int32)
    mate_basis = got[own.size + pos_len:].reshape(basis.shape).astype(basis.dtype)
    low_core = col_index % 2 == 0
    pair_position = jnp.where(low_core, jnp.concatenate([position, mate_position], 1), jnp.concatenate([mate_position, position], 1))
    pair_basis = jnp.where(low_core, jnp.concatenate([basis, mate_basis], 1), jnp.concatenate([mate_basis, basis], 1))
    wanted = pair_position.reshape(-1)
    looked = look_up(own, col_index) + look_up(other, col_index ^ 1)
    held = jnp.where(low_core, jnp.concatenate([own, other], -1), jnp.concatenate([other, own], -1))
    step = 2
    while step < col_total:
        other = lax.ppermute(held, "col", perm=[(i, i ^ step) for i in range(col_total)])
        looked = looked + look_up(other, ((col_index // step) ^ 1) * step)
        low_half = (col_index // step) % 2 == 0
        held = jnp.where(low_half, jnp.concatenate([held, other], -1), jnp.concatenate([other, held], -1))
        step *= 2
    value_data = held.reshape(2, col_total, own_len)[:, :, pole_dev:].reshape(2, -1)
    row_total = lax.axis_size("row")
    step = 1
    while step < row_total:
        looked = looked + lax.ppermute(looked, "row", perm=[(i, i ^ step) for i in range(row_total)])
        step *= 2
    child_id = lax.axis_index("row") // (row_total // 2)
    own_cols = pair_position.shape[1]
    own_poles = lax.dynamic_slice_in_dim(looked, child_id * own_cols, own_cols, 1)
    pole_at = own_poles[0]
    live_at = own_poles[1]
    chunk = 512
    contract = (((1,), (1,)), ((), ()))

    blocks = value_data.reshape(2, col_total, -1)
    value_data = jnp.concatenate([blocks[:, b] for b in bit_reversed(col_total)], 1)

    def compute_range(inputs, offset, width):
        pole_at, live_at, value_data = inputs
        parts = []
        for start in range(0, width, chunk):
            values = lax.dynamic_slice_in_dim(value_data, offset + start, chunk, 1)
            upper, lower = split_parts(cauchy_tile_t(pole_at, live_at, values[0], values[1]))
            first_term = lax.dot_general(pair_basis, upper, contract, preferred_element_type=jnp.float32)
            second_term = lax.dot_general(pair_basis, lower, contract, preferred_element_type=jnp.float32)
            parts.append(first_term + second_term)
        return jnp.concatenate(parts, 1)

    half_new = value_data.shape[1] // 2
    summed = reduce_by_halves(compute_range, (col_index % 2) * half_new, half_new, "col", (pole_at, live_at, value_data), 2)
    return summed.astype(jnp.bfloat16)


def solution(mesh):
    placed = (
        P("row", "col"),
        P(None, "col"),
        P(("row", "col")),
        P(("row", "col")),
        P(("row", "col")),
        P("col"),
        P("col"),
    )
    return jax.shard_map(
        per_device, mesh=mesh, in_specs=placed, out_specs=P("row", "col"), check_vma=False
    )
```

```python
import jax
import jax.numpy as jnp
from jax import lax
from jax.sharding import PartitionSpec as P


def cauchy_tile_t(pole_row, live_row, value_at, scale_at):
    return live_row[None, :] / (pole_row[None, :] - value_at[:, None]) * scale_at[:, None]


def gather_by_pairs(block, axis):
    size = lax.axis_size(axis)
    index = lax.axis_index(axis)
    held = block
    step = 1
    while step < size:
        other = lax.ppermute(held, axis, perm=[(i, i ^ step) for i in range(size)])
        low_half = (index // step) % 2 == 0
        held = jnp.where(low_half, jnp.concatenate([held, other], -1), jnp.concatenate([other, held], -1))
        step *= 2
    return held


def reduce_by_halves(compute_range, total, axis, inputs):
    size = lax.axis_size(axis)
    index = lax.axis_index(axis)
    step = 1
    width = total // 2
    bit = index % 2
    sent = compute_range(inputs, (1 - bit) * width, width)
    sent, inputs = lax.optimization_barrier((sent, inputs))
    got = lax.ppermute(sent, axis, perm=[(i, i ^ step) for i in range(size)])
    held = compute_range(inputs, bit * width, width) + got
    step *= 2
    while step < size:
        width //= 2
        bit = (index // step) % 2
        sent = lax.dynamic_slice_in_dim(held, (1 - bit) * width, width, -1)
        kept = lax.dynamic_slice_in_dim(held, bit * width, width, -1)
        held = kept + lax.ppermute(sent, axis, perm=[(i, i ^ step) for i in range(size)])
        step *= 2
    return held


def bit_reversed(count):
    width = count.bit_length() - 1
    return [int(format(i, "0%db" % width)[::-1], 2) for i in range(count)]


def per_device(basis, position, poles, weights, kept, eigenvalues, scales):
    live_weight = weights * kept.astype(jnp.float32)
    col_total = lax.axis_size("col")
    pole_dev = poles.shape[0]
    own = jnp.concatenate([jnp.stack([poles, live_weight]), jnp.stack([eigenvalues, scales])], 1)
    own_len = own.shape[1]
    col_index = lax.axis_index("col")
    row_base = lax.axis_index("row") * (col_total * pole_dev)
    wanted = position.reshape(-1)

    def look_up(block, first_col):
        count = block.shape[1] // own_len
        part = block.reshape(2, count, own_len)[:, :, :pole_dev].reshape(2, -1)
        pieces = []
        rest = part
        for _ in range(3):
            piece = lax.optimization_barrier(rest.astype(jnp.bfloat16))
            rest = rest - piece.astype(jnp.float32)
            pieces.append(piece)
        table = jnp.concatenate(pieces, 0)
        local = wanted - (row_base + first_col * pole_dev)
        found_all = []
        span = 512
        for begin in range(0, local.shape[0], span):
            hits = local[begin:begin + span, None] == lax.iota(jnp.int32, part.shape[1])[None, :]
            found = lax.dot_general(table, hits.astype(jnp.bfloat16), (((1,), (1,)), ((), ())), preferred_element_type=jnp.float32)
            found_all.append((found[0:2] + found[2:4]) + found[4:6])
        return jnp.concatenate(found_all, 1)

    looked = look_up(own, col_index)
    held = own
    step = 1
    while step < col_total:
        other = lax.ppermute(held, "col", perm=[(i, i ^ step) for i in range(col_total)])
        looked = looked + look_up(other, ((col_index // step) ^ 1) * step)
        low_half = (col_index // step) % 2 == 0
        held = jnp.where(low_half, jnp.concatenate([held, other], -1), jnp.concatenate([other, held], -1))
        step *= 2
    value_data = held.reshape(2, col_total, own_len)[:, :, pole_dev:].reshape(2, -1)
    row_total = lax.axis_size("row")
    step = 1
    while step < row_total:
        looked = looked + lax.ppermute(looked, "row", perm=[(i, i ^ step) for i in range(row_total)])
        step *= 2
    child_id = lax.axis_index("row") // (row_total // 2)
    own_cols = position.shape[1]
    own_poles = lax.dynamic_slice_in_dim(looked, child_id * own_cols, own_cols, 1)
    pole_at = own_poles[0]
    live_at = own_poles[1]
    chunk = 512
    contract = (((1,), (1,)), ((), ()))

    blocks = value_data.reshape(2, col_total, -1)
    value_data = jnp.concatenate([blocks[:, b] for b in bit_reversed(col_total)], 1)

    basis_wide = basis.astype(jnp.float32)

    def compute_range(inputs, offset, width):
        pole_at, live_at, value_data = inputs
        parts = []
        for start in range(0, width, chunk):
            values = lax.dynamic_slice_in_dim(value_data, offset + start, chunk, 1)
            cauchy = cauchy_tile_t(pole_at, live_at, values[0], values[1])
            parts.append(lax.dot_general(basis_wide, cauchy, contract, precision=lax.Precision.HIGH, preferred_element_type=jnp.float32))
        return jnp.concatenate(parts, 1)

    summed = reduce_by_halves(compute_range, value_data.shape[1], "col", (pole_at, live_at, value_data))
    return summed.astype(jnp.bfloat16)


def solution(mesh):
    placed = (
        P("row", "col"),
        P(None, "col"),
        P(("row", "col")),
        P(("row", "col")),
        P(("row", "col")),
        P("col"),
        P("col"),
    )
    return jax.shard_map(
        per_device, mesh=mesh, in_specs=placed, out_specs=P("row", "col"), check_vma=False
    )
```

```python
import jax
import jax.numpy as jnp
from jax import lax
from jax.sharding import PartitionSpec as P


def cauchy_tile_t(pole_row, live_row, value_at, scale_at):
    return live_row[None, :] / (pole_row[None, :] - value_at[:, None]) * scale_at[:, None]


def gather_by_pairs(block, axis):
    size = lax.axis_size(axis)
    index = lax.axis_index(axis)
    held = block
    step = 1
    while step < size:
        other = lax.ppermute(held, axis, perm=[(i, i ^ step) for i in range(size)])
        low_half = (index // step) % 2 == 0
        held = jnp.where(low_half, jnp.concatenate([held, other], -1), jnp.concatenate([other, held], -1))
        step *= 2
    return held


def reduce_by_halves(compute_range, total, axis, inputs):
    size = lax.axis_size(axis)
    index = lax.axis_index(axis)
    step = 1
    width = total // 2
    bit = index % 2
    sent = compute_range(inputs, (1 - bit) * width, width)
    sent, inputs = lax.optimization_barrier((sent, inputs))
    got = lax.ppermute(sent, axis, perm=[(i, i ^ step) for i in range(size)])
    held = compute_range(inputs, bit * width, width) + got
    step *= 2
    while step < size:
        width //= 2
        bit = (index // step) % 2
        sent = lax.dynamic_slice_in_dim(held, (1 - bit) * width, width, -1)
        kept = lax.dynamic_slice_in_dim(held, bit * width, width, -1)
        held = kept + lax.ppermute(sent, axis, perm=[(i, i ^ step) for i in range(size)])
        step *= 2
    return held


def bit_reversed(count):
    width = count.bit_length() - 1
    return [int(format(i, "0%db" % width)[::-1], 2) for i in range(count)]


def per_device(basis, position, poles, weights, kept, eigenvalues, scales):
    live_weight = weights * kept.astype(jnp.float32)
    col_total = lax.axis_size("col")
    pole_dev = poles.shape[0]
    own = jnp.concatenate([jnp.stack([poles, live_weight]), jnp.stack([eigenvalues, scales])], 1)
    own_len = own.shape[1]
    col_index = lax.axis_index("col")
    row_base = lax.axis_index("row") * (col_total * pole_dev)
    wanted = position.reshape(-1)

    def look_up(block, first_col):
        count = block.shape[1] // own_len
        part = block.reshape(2, count, own_len)[:, :, :pole_dev].reshape(2, -1)
        pieces = []
        rest = part
        for _ in range(3):
            piece = lax.optimization_barrier(rest.astype(jnp.bfloat16))
            rest = rest - piece.astype(jnp.float32)
            pieces.append(piece)
        table = jnp.concatenate(pieces, 0)
        local = wanted - (row_base + first_col * pole_dev)
        found_all = []
        span = 512
        for begin in range(0, local.shape[0], span):
            hits = local[begin:begin + span, None] == lax.iota(jnp.int32, part.shape[1])[None, :]
            found = lax.dot_general(table, hits.astype(jnp.bfloat16), (((1,), (1,)), ((), ())), preferred_element_type=jnp.float32)
            found_all.append((found[0:2] + found[2:4]) + found[4:6])
        return jnp.concatenate(found_all, 1)

    looked = look_up(own, col_index)
    held = own
    step = 1
    while step < col_total:
        other = lax.ppermute(held, "col", perm=[(i, i ^ step) for i in range(col_total)])
        looked = looked + look_up(other, ((col_index // step) ^ 1) * step)
        low_half = (col_index // step) % 2 == 0
        held = jnp.where(low_half, jnp.concatenate([held, other], -1), jnp.concatenate([other, held], -1))
        step *= 2
    value_data = held.reshape(2, col_total, own_len)[:, :, pole_dev:].reshape(2, -1)
    row_total = lax.axis_size("row")
    half_rows = row_total // 2
    child_id = lax.axis_index("row") // half_rows
    own_cols = position.shape[1]
    mine = lax.dynamic_slice_in_dim(looked, child_id * own_cols, own_cols, 1)
    theirs = lax.dynamic_slice_in_dim(looked, (1 - child_id) * own_cols, own_cols, 1)
    looked = mine + lax.ppermute(theirs, "row", perm=[(i, i ^ half_rows) for i in range(row_total)])
    step = 1
    while step < half_rows:
        looked = looked + lax.ppermute(looked, "row", perm=[(i, i ^ step) for i in range(row_total)])
        step *= 2
    pole_at = looked[0]
    live_at = looked[1]
    chunk = 1024
    contract = (((1,), (1,)), ((), ()))

    blocks = value_data.reshape(2, col_total, -1)
    value_data = jnp.concatenate([blocks[:, b] for b in bit_reversed(col_total)], 1)

    basis_wide = basis.astype(jnp.float32)

    def compute_range(inputs, offset, width):
        pole_at, live_at, value_data = inputs
        parts = []
        for start in range(0, width, chunk):
            values = lax.dynamic_slice_in_dim(value_data, offset + start, chunk, 1)
            cauchy = cauchy_tile_t(pole_at, live_at, values[0], values[1])
            parts.append(lax.dot_general(basis_wide, cauchy, contract, precision=lax.Precision.HIGH, preferred_element_type=jnp.float32))
        return jnp.concatenate(parts, 1)

    summed = reduce_by_halves(compute_range, value_data.shape[1], "col", (pole_at, live_at, value_data))
    return summed.astype(jnp.bfloat16)


def solution(mesh):
    placed = (
        P("row", "col"),
        P(None, "col"),
        P(("row", "col")),
        P(("row", "col")),
        P(("row", "col")),
        P("col"),
        P("col"),
    )
    return jax.shard_map(
        per_device, mesh=mesh, in_specs=placed, out_specs=P("row", "col"), check_vma=False
    )
```

```python
import jax
import jax.numpy as jnp
from jax import lax
from jax.sharding import PartitionSpec as P


def cauchy_tile_t(pole_row, live_row, value_at, scale_at):
    return live_row[None, :] / (pole_row[None, :] - value_at[:, None]) * scale_at[:, None]


def gather_by_pairs(block, axis):
    size = lax.axis_size(axis)
    index = lax.axis_index(axis)
    held = block
    step = 1
    while step < size:
        other = lax.ppermute(held, axis, perm=[(i, i ^ step) for i in range(size)])
        low_half = (index // step) % 2 == 0
        held = jnp.where(low_half, jnp.concatenate([held, other], -1), jnp.concatenate([other, held], -1))
        step *= 2
    return held


def reduce_by_halves(compute_range, total, axis, inputs):
    size = lax.axis_size(axis)
    index = lax.axis_index(axis)
    step = 1
    width = total // 2
    bit = index % 2
    sent = compute_range(inputs, (1 - bit) * width, width)
    sent, inputs = lax.optimization_barrier((sent, inputs))
    got = lax.ppermute(sent, axis, perm=[(i, i ^ step) for i in range(size)])
    held = compute_range(inputs, bit * width, width) + got
    step *= 2
    while step < size:
        width //= 2
        bit = (index // step) % 2
        sent = lax.dynamic_slice_in_dim(held, (1 - bit) * width, width, -1)
        kept = lax.dynamic_slice_in_dim(held, bit * width, width, -1)
        held = kept + lax.ppermute(sent, axis, perm=[(i, i ^ step) for i in range(size)])
        step *= 2
    return held


def bit_reversed(count):
    width = count.bit_length() - 1
    return [int(format(i, "0%db" % width)[::-1], 2) for i in range(count)]


def per_device(basis, position, poles, weights, kept, eigenvalues, scales):
    live_weight = weights * kept.astype(jnp.float32)
    col_total = lax.axis_size("col")
    pole_dev = poles.shape[0]
    own = jnp.concatenate([jnp.stack([poles, live_weight]), jnp.stack([eigenvalues, scales])], 1)
    own_len = own.shape[1]
    col_index = lax.axis_index("col")
    row_base = lax.axis_index("row") * (col_total * pole_dev)
    wanted = position.reshape(-1)

    def look_up(block, first_col):
        count = block.shape[1] // own_len
        part = block.reshape(2, count, own_len)[:, :, :pole_dev].reshape(2, -1)
        pieces = []
        rest = part
        for _ in range(3):
            piece = lax.optimization_barrier(rest.astype(jnp.bfloat16))
            rest = rest - piece.astype(jnp.float32)
            pieces.append(piece)
        table = jnp.concatenate(pieces, 0)
        local = wanted - (row_base + first_col * pole_dev)
        found_all = []
        span = 512
        for begin in range(0, local.shape[0], span):
            hits = local[begin:begin + span, None] == lax.iota(jnp.int32, part.shape[1])[None, :]
            found = lax.dot_general(table, hits.astype(jnp.bfloat16), (((1,), (1,)), ((), ())), preferred_element_type=jnp.float32)
            found_all.append((found[0:2] + found[2:4]) + found[4:6])
        return jnp.concatenate(found_all, 1)

    looked = look_up(own, col_index)
    held = own
    step = 1
    while step < col_total:
        other = lax.ppermute(held, "col", perm=[(i, i ^ step) for i in range(col_total)])
        looked = looked + look_up(other, ((col_index // step) ^ 1) * step)
        low_half = (col_index // step) % 2 == 0
        held = jnp.where(low_half, jnp.concatenate([held, other], -1), jnp.concatenate([other, held], -1))
        step *= 2
    value_data = held.reshape(2, col_total, own_len)[:, :, pole_dev:].reshape(2, -1)
    row_total = lax.axis_size("row")
    half_rows = row_total // 2
    child_id = lax.axis_index("row") // half_rows
    own_cols = position.shape[1]
    mine = lax.dynamic_slice_in_dim(looked, child_id * own_cols, own_cols, 1)
    theirs = lax.dynamic_slice_in_dim(looked, (1 - child_id) * own_cols, own_cols, 1)
    looked = mine + lax.ppermute(theirs, "row", perm=[(i, i ^ half_rows) for i in range(row_total)])
    step = 1
    while step < half_rows:
        looked = looked + lax.ppermute(looked, "row", perm=[(i, i ^ step) for i in range(row_total)])
        step *= 2
    pole_at = looked[0]
    live_at = looked[1]
    chunk = 2048
    contract = (((1,), (1,)), ((), ()))

    blocks = value_data.reshape(2, col_total, -1)
    value_data = jnp.concatenate([blocks[:, b] for b in bit_reversed(col_total)], 1)

    basis_wide = basis.astype(jnp.float32)

    def compute_range(inputs, offset, width):
        pole_at, live_at, value_data = inputs
        parts = []
        for start in range(0, width, chunk):
            values = lax.dynamic_slice_in_dim(value_data, offset + start, chunk, 1)
            cauchy = cauchy_tile_t(pole_at, live_at, values[0], values[1])
            parts.append(lax.dot_general(basis_wide, cauchy, contract, precision=lax.Precision.HIGH, preferred_element_type=jnp.float32))
        return jnp.concatenate(parts, 1)

    summed = reduce_by_halves(compute_range, value_data.shape[1], "col", (pole_at, live_at, value_data))
    return summed.astype(jnp.bfloat16)


def solution(mesh):
    placed = (
        P("row", "col"),
        P(None, "col"),
        P(("row", "col")),
        P(("row", "col")),
        P(("row", "col")),
        P("col"),
        P("col"),
    )
    return jax.shard_map(
        per_device, mesh=mesh, in_specs=placed, out_specs=P("row", "col"), check_vma=False
    )
```

```python
import jax
import jax.numpy as jnp
from jax import lax
from jax.sharding import PartitionSpec as P


def cauchy_tile_t(pole_row, live_row, value_at, scale_at):
    return live_row[None, :] / (pole_row[None, :] - value_at[:, None]) * scale_at[:, None]


def gather_by_pairs(block, axis):
    size = lax.axis_size(axis)
    index = lax.axis_index(axis)
    held = block
    step = 1
    while step < size:
        other = lax.ppermute(held, axis, perm=[(i, i ^ step) for i in range(size)])
        low_half = (index // step) % 2 == 0
        held = jnp.where(low_half, jnp.concatenate([held, other], -1), jnp.concatenate([other, held], -1))
        step *= 2
    return held


def reduce_by_halves(compute_range, total, axis, inputs):
    size = lax.axis_size(axis)
    index = lax.axis_index(axis)
    step = 1
    width = total // 2
    bit = index % 2
    sent = compute_range(inputs, (1 - bit) * width, width)
    sent, inputs = lax.optimization_barrier((sent, inputs))
    pending = lax.ppermute(sent, axis, perm=[(i, i ^ step) for i in range(size)])
    low = bit * width
    step *= 2
    while step < size:
        width //= 2
        bit = (index // step) % 2
        sent = compute_range(inputs, low + (1 - bit) * width, width)
        sent = sent + lax.dynamic_slice_in_dim(pending, (1 - bit) * width, width, -1)
        kept = lax.dynamic_slice_in_dim(pending, bit * width, width, -1)
        sent, inputs = lax.optimization_barrier((sent, inputs))
        pending = kept + lax.ppermute(sent, axis, perm=[(i, i ^ step) for i in range(size)])
        low = low + bit * width
        step *= 2
    return compute_range(inputs, low, width) + pending


def bit_reversed(count):
    width = count.bit_length() - 1
    return [int(format(i, "0%db" % width)[::-1], 2) for i in range(count)]


def per_device(basis, position, poles, weights, kept, eigenvalues, scales):
    live_weight = weights * kept.astype(jnp.float32)
    col_total = lax.axis_size("col")
    pole_dev = poles.shape[0]
    own = jnp.concatenate([jnp.stack([poles, live_weight]), jnp.stack([eigenvalues, scales])], 1)
    own_len = own.shape[1]
    col_index = lax.axis_index("col")
    row_base = lax.axis_index("row") * (col_total * pole_dev)
    wanted = position.reshape(-1)

    def look_up(block, first_col):
        count = block.shape[1] // own_len
        part = block.reshape(2, count, own_len)[:, :, :pole_dev].reshape(2, -1)
        pieces = []
        rest = part
        for _ in range(3):
            piece = lax.optimization_barrier(rest.astype(jnp.bfloat16))
            rest = rest - piece.astype(jnp.float32)
            pieces.append(piece)
        table = jnp.concatenate(pieces, 0)
        local = wanted - (row_base + first_col * pole_dev)
        found_all = []
        span = 512
        for begin in range(0, local.shape[0], span):
            hits = local[begin:begin + span, None] == lax.iota(jnp.int32, part.shape[1])[None, :]
            found = lax.dot_general(table, hits.astype(jnp.bfloat16), (((1,), (1,)), ((), ())), preferred_element_type=jnp.float32)
            found_all.append((found[0:2] + found[2:4]) + found[4:6])
        return jnp.concatenate(found_all, 1)

    looked = look_up(own, col_index)
    held = own
    step = 1
    while step < col_total:
        other = lax.ppermute(held, "col", perm=[(i, i ^ step) for i in range(col_total)])
        looked = looked + look_up(other, ((col_index // step) ^ 1) * step)
        low_half = (col_index // step) % 2 == 0
        held = jnp.where(low_half, jnp.concatenate([held, other], -1), jnp.concatenate([other, held], -1))
        step *= 2
    value_data = held.reshape(2, col_total, own_len)[:, :, pole_dev:].reshape(2, -1)
    row_total = lax.axis_size("row")
    half_rows = row_total // 2
    child_id = lax.axis_index("row") // half_rows
    own_cols = position.shape[1]
    mine = lax.dynamic_slice_in_dim(looked, child_id * own_cols, own_cols, 1)
    theirs = lax.dynamic_slice_in_dim(looked, (1 - child_id) * own_cols, own_cols, 1)
    looked = mine + lax.ppermute(theirs, "row", perm=[(i, i ^ half_rows) for i in range(row_total)])
    step = 1
    while step < half_rows:
        looked = looked + lax.ppermute(looked, "row", perm=[(i, i ^ step) for i in range(row_total)])
        step *= 2
    pole_at = looked[0]
    live_at = looked[1]
    chunk = 1024
    contract = (((1,), (1,)), ((), ()))

    blocks = value_data.reshape(2, col_total, -1)
    value_data = jnp.concatenate([blocks[:, b] for b in bit_reversed(col_total)], 1)

    basis_wide = basis.astype(jnp.float32)

    def compute_range(inputs, offset, width):
        pole_at, live_at, value_data = inputs
        parts = []
        size = min(chunk, width)
        for start in range(0, width, size):
            values = lax.dynamic_slice_in_dim(value_data, offset + start, size, 1)
            cauchy = cauchy_tile_t(pole_at, live_at, values[0], values[1])
            parts.append(lax.dot_general(basis_wide, cauchy, contract, precision=lax.Precision.HIGH, preferred_element_type=jnp.float32))
        return jnp.concatenate(parts, 1)

    summed = reduce_by_halves(compute_range, value_data.shape[1], "col", (pole_at, live_at, value_data))
    return summed.astype(jnp.bfloat16)


def solution(mesh):
    placed = (
        P("row", "col"),
        P(None, "col"),
        P(("row", "col")),
        P(("row", "col")),
        P(("row", "col")),
        P("col"),
        P("col"),
    )
    return jax.shard_map(
        per_device, mesh=mesh, in_specs=placed, out_specs=P("row", "col"), check_vma=False
    )
```

```python
import jax
import jax.numpy as jnp
from jax import lax
from jax.sharding import PartitionSpec as P


def cauchy_tile_t(pole_row, live_row, value_at, scale_at):
    return live_row[None, :] / (pole_row[None, :] - value_at[:, None]) * scale_at[:, None]


def gather_by_pairs(block, axis):
    size = lax.axis_size(axis)
    index = lax.axis_index(axis)
    held = block
    step = 1
    while step < size:
        other = lax.ppermute(held, axis, perm=[(i, i ^ step) for i in range(size)])
        low_half = (index // step) % 2 == 0
        held = jnp.where(low_half, jnp.concatenate([held, other], -1), jnp.concatenate([other, held], -1))
        step *= 2
    return held


def reduce_by_halves(compute_range, total, axis, inputs):
    size = lax.axis_size(axis)
    index = lax.axis_index(axis)
    step = 1
    width = total // 2
    bit = index % 2
    sent = compute_range(inputs, (1 - bit) * width, width)
    sent, inputs = lax.optimization_barrier((sent, inputs))
    got = lax.ppermute(sent, axis, perm=[(i, i ^ step) for i in range(size)])
    held = compute_range(inputs, bit * width, width) + got
    step *= 2
    while step < size:
        width //= 2
        bit = (index // step) % 2
        sent = lax.dynamic_slice_in_dim(held, (1 - bit) * width, width, -1)
        kept = lax.dynamic_slice_in_dim(held, bit * width, width, -1)
        held = kept + lax.ppermute(sent, axis, perm=[(i, i ^ step) for i in range(size)])
        step *= 2
    return held


def bit_reversed(count):
    width = count.bit_length() - 1
    return [int(format(i, "0%db" % width)[::-1], 2) for i in range(count)]


def per_device(basis, position, poles, weights, kept, eigenvalues, scales):
    live_weight = weights * kept.astype(jnp.float32)
    col_total = lax.axis_size("col")
    pole_dev = poles.shape[0]
    own = jnp.concatenate([jnp.stack([poles, live_weight]), jnp.stack([eigenvalues, scales])], 1)
    own_len = own.shape[1]
    col_index = lax.axis_index("col")
    row_base = lax.axis_index("row") * (col_total * pole_dev)
    wanted = position.reshape(-1)

    def look_up(block, first_col):
        count = block.shape[1] // own_len
        part = block.reshape(2, count, own_len)[:, :, :pole_dev].reshape(2, -1)
        pieces = []
        rest = part
        for _ in range(3):
            piece = lax.optimization_barrier(rest.astype(jnp.bfloat16))
            rest = rest - piece.astype(jnp.float32)
            pieces.append(piece)
        table = jnp.concatenate(pieces, 0)
        local = wanted - (row_base + first_col * pole_dev)
        found_all = []
        span = 512
        for begin in range(0, local.shape[0], span):
            hits = local[begin:begin + span, None] == lax.iota(jnp.int32, part.shape[1])[None, :]
            found = lax.dot_general(table, hits.astype(jnp.bfloat16), (((1,), (1,)), ((), ())), preferred_element_type=jnp.float32)
            found_all.append((found[0:2] + found[2:4]) + found[4:6])
        return jnp.concatenate(found_all, 1)

    looked = look_up(own, col_index)
    held = own
    step = 1
    while step < col_total:
        other = lax.ppermute(held, "col", perm=[(i, i ^ step) for i in range(col_total)])
        looked = looked + look_up(other, ((col_index // step) ^ 1) * step)
        low_half = (col_index // step) % 2 == 0
        held = jnp.where(low_half, jnp.concatenate([held, other], -1), jnp.concatenate([other, held], -1))
        step *= 2
    value_data = held.reshape(2, col_total, own_len)[:, :, pole_dev:].reshape(2, -1)
    row_total = lax.axis_size("row")
    half_rows = row_total // 2
    child_id = lax.axis_index("row") // half_rows
    own_cols = position.shape[1]
    mine = lax.dynamic_slice_in_dim(looked, child_id * own_cols, own_cols, 1)
    theirs = lax.dynamic_slice_in_dim(looked, (1 - child_id) * own_cols, own_cols, 1)
    fast = row_total // 8
    mirror = [(row_total // fast - 1 - i // fast) * fast + i % fast for i in range(row_total)]
    looked = mine + lax.ppermute(theirs, "row", perm=[(i, mirror[i]) for i in range(row_total)])
    step = 1
    while step < half_rows:
        looked = looked + lax.ppermute(looked, "row", perm=[(i, i ^ step) for i in range(row_total)])
        step *= 2
    pole_at = looked[0]
    live_at = looked[1]
    chunk = 1024
    contract = (((1,), (1,)), ((), ()))

    blocks = value_data.reshape(2, col_total, -1)
    value_data = jnp.concatenate([blocks[:, b] for b in bit_reversed(col_total)], 1)

    basis_wide = basis.astype(jnp.float32)

    def compute_range(inputs, offset, width):
        pole_at, live_at, value_data = inputs
        parts = []
        for start in range(0, width, chunk):
            values = lax.dynamic_slice_in_dim(value_data, offset + start, chunk, 1)
            cauchy = cauchy_tile_t(pole_at, live_at, values[0], values[1])
            parts.append(lax.dot_general(basis_wide, cauchy, contract, precision=lax.Precision.HIGH, preferred_element_type=jnp.float32))
        return jnp.concatenate(parts, 1)

    summed = reduce_by_halves(compute_range, value_data.shape[1], "col", (pole_at, live_at, value_data))
    return summed.astype(jnp.bfloat16)


def solution(mesh):
    placed = (
        P("row", "col"),
        P(None, "col"),
        P(("row", "col")),
        P(("row", "col")),
        P(("row", "col")),
        P("col"),
        P("col"),
    )
    return jax.shard_map(
        per_device, mesh=mesh, in_specs=placed, out_specs=P("row", "col"), check_vma=False
    )
```
